256 devices in a mesh: prow: 8 (over y, x_hi), pcol: 32 (over x_lo, z, core).
Axes of the slice: x: 4 (x_hi: 2, x_lo: 2; x = x_hi * 2 + x_lo), y: 4, z: 8, core: 2. Of those that a mesh axis runs over, the one named last changes fastest.
Arguments:
- covariance: float32 [8, 8, 256, 32, 2, 256], P('prow', None, None, 'pcol'), may hold values from 0 to 3, as said below
Outputs:
- factored: float32 [8, 8, 256, 32, 2, 256], P('prow', None, None, 'pcol')
The draws below stay inside these ranges and needn't reach their ends.
Inputs may be any that keep to these rules, and one draw needn't show every extreme that they name: covariance is symmetric and positive definite.
All inputs are finite; a program needn't handle non-finite values.
Results may differ from the reference program's by a relative error of at most 0.0003.
Values sent between devices are 32-bit elements; how exact they have to be, the bound alone decides.
No kernel may reach another device: no remote copies, remote signals or barrier semaphores. Data moves between devices by JAX's collectives and lax.ppermute only.
A program may use at most 64 MiB of HBM per device.

```python
import jax
import jax.numpy as jnp
from jax import lax

N = 16384
NB = 256
PANELS = 2
RT = 8
CT = 2
N_PROW = 8
N_PCOL = 32


def draw_covariance(key, part):
    key_points, key_scale, key_nugget = jax.random.split(jax.random.fold_in(key, 71), 3)
    points = jax.random.uniform(key_points, (N, 6), jnp.float32)
    spread = jax.random.uniform(key_scale, (N,), jnp.float32, 0.6, 1.5)
    nugget = jax.random.uniform(key_nugget, (N,), jnp.float32, 0.2, 0.6)
    row_pts = points.reshape(RT, N_PROW, NB, 6).transpose(1, 0, 2, 3)
    col_pts = points.reshape(CT, N_PCOL, NB, 6).transpose(1, 0, 2, 3)
    squared = jnp.zeros((N_PROW, RT, NB, N_PCOL, CT, NB), jnp.float32)
    for coord in range(6):
        diff = row_pts[:, :, :, coord][:, :, :, None, None, None] - col_pts[:, :, :, coord][None, None, None]
        squared = squared + diff * diff
    scaled = jnp.sqrt(squared) * 3.0 ** 0.5
    kernel = (1.0 + scaled) * jnp.exp(-scaled)
    row_spread = spread.reshape(RT, N_PROW, NB).transpose(1, 0, 2)[:, :, :, None, None, None]
    col_spread = spread.reshape(CT, N_PCOL, NB).transpose(1, 0, 2)[None, None, None]
    row_ids = jnp.arange(N, dtype=jnp.int32).reshape(RT, N_PROW, NB).transpose(1, 0, 2)[:, :, :, None, None, None]
    col_ids = jnp.arange(N, dtype=jnp.int32).reshape(CT, N_PCOL, NB).transpose(1, 0, 2)[None, None, None]
    row_nugget = nugget.reshape(RT, N_PROW, NB).transpose(1, 0, 2)[:, :, :, None, None, None]
    return row_spread * col_spread * kernel + jnp.where(row_ids == col_ids, row_nugget, 0.0)


def setup_inputs(seed: int = 0) -> dict:
    splits = jax.random.split(jax.random.key(seed), 2)
    covariance = draw_covariance(jax.random.fold_in(splits[1], 71), 0)
    return {"covariance": covariance}


def to_full(tiles):
    return tiles.transpose(1, 0, 2, 4, 3, 5).reshape(N, N)

def to_tiles(full):
    return full.reshape(RT, N_PROW, NB, CT, N_PCOL, NB).transpose(1, 0, 2, 4, 3, 5)

def reference(covariance):
    full = to_full(covariance)
    for panel in range(PANELS):
        lower = panel * NB
        upper = lower + NB
        factor = jnp.linalg.cholesky(full[lower:upper, lower:upper])
        below = jax.scipy.linalg.solve_triangular(factor, full[upper:, lower:upper].T, lower=True).T
        update = jnp.dot(below, below.T, precision=lax.Precision.HIGHEST)
        full = full.at[upper:, upper:].add(-update)
        full = full.at[lower:upper, lower:upper].set(factor)
        full = full.at[upper:, lower:upper].set(below)
        full = full.at[lower:upper, upper:].set(jnp.zeros((NB, N - upper), jnp.float32))
    return to_tiles(full)
```

```python
import jax
import jax.numpy as jnp
from jax import lax
from jax.sharding import PartitionSpec as P

PANELS = 2
HI = lax.Precision.HIGHEST


def prow_from_first_two(x, prows):
    me = lax.axis_index("prow")
    got = [x]
    for d in range(1, prows):
        got.append(lax.ppermute(x, "prow", [(0, d), (1, (1 + d) % prows)]))
    stack = jnp.stack(got)
    return stack[me], stack[(me + prows - 1) % prows]


def pcol_tree_rounds(pcols):
    zs = pcols // 4

    def idx(x, z, core):
        return (x * zs + z % zs) * 2 + core

    rounds = []
    a_have = [(0, 0)]
    b_have = [(0, 0)]
    steps_a = [("x", 0), ("z", zs // 2)]
    steps_b = [("z", zs // 2), ("x", 0)]
    s = zs // 4
    while s >= 1:
        steps_a.append(("z", s))
        steps_b.append(("z", -s))
        s //= 2
    for (ka, da), (kb, db) in zip(steps_a, steps_b):
        pairs = []
        new_a = []
        for x, z in a_have:
            t = (1 - x, z) if ka == "x" else (x, (z + da) % zs)
            pairs.append((idx(x, z, 0), idx(t[0], t[1], 0)))
            new_a.append(t)
        new_b = []
        for x, z in b_have:
            t = (1 - x, z) if kb == "x" else (x, (z + db) % zs)
            pairs.append((idx(x, z, 1), idx(t[0], t[1], 1)))
            new_b.append(t)
        a_have += new_a
        b_have += new_b
        rounds.append(pairs)
    return rounds


def pcol_broadcast_pair(buf, pcols):
    me = lax.axis_index("pcol")
    for pairs in pcol_tree_rounds(pcols):
        got = lax.ppermute(buf, "pcol", pairs)
        targets = jnp.array([t for _, t in pairs], jnp.int32)
        hit = jnp.any(targets == me)
        buf = jnp.where(hit, got, buf)
    other = lax.ppermute(buf, "pcol", [(i, i ^ 1) for i in range(pcols)])
    core0 = (me % 2) == 0
    return jnp.where(core0, buf, other), jnp.where(core0, other, buf)


def per_device(covariance):
    prows = lax.axis_size("prow")
    pcols = lax.axis_size("pcol")
    p = lax.axis_index("prow")
    q = lax.axis_index("pcol")
    rt = covariance.shape[1]
    tile = covariance.shape[2]
    ct = covariance.shape[4]
    nb = PANELS * tile
    tiles = covariance.reshape(rt, tile, ct, tile)

    t0, t1 = prow_from_first_two(tiles[0], prows)

    col0, col1 = pcol_broadcast_pair(tiles[:, :, 0, :], pcols)

    diag_a, diag_b = pcol_broadcast_pair(jnp.stack([t0[:, 0, :], t1[:, 0, :]]), pcols)
    block = jnp.concatenate(
        [
            jnp.concatenate([diag_a[0], diag_b[0]], axis=1),
            jnp.concatenate([diag_a[1], diag_b[1]], axis=1),
        ],
        axis=0,
    )
    factor = jnp.tril(jnp.linalg.cholesky(block))
    inverse = jax.scipy.linalg.solve_triangular(
        factor, jnp.eye(nb, dtype=factor.dtype), lower=True
    )

    rows_panel = jnp.concatenate([col0, col1], axis=-1)
    cols_panel = jnp.concatenate(
        [jnp.transpose(t0, (1, 2, 0)), jnp.transpose(t1, (1, 2, 0))], axis=-1
    )
    rows_solved = jnp.einsum("rak,bk->rab", rows_panel, inverse, precision=HI)
    cols_solved = jnp.einsum("cak,bk->cab", cols_panel, inverse, precision=HI)
    update = tiles - jnp.einsum("rak,cbk->racb", rows_solved, cols_solved, precision=HI)

    row_index = jnp.arange(rt, dtype=jnp.int32) * prows + p
    col_index = jnp.arange(ct, dtype=jnp.int32) * pcols + q
    trailing = (row_index >= PANELS)[:, None, None, None] & (col_index >= PANELS)[
        None, None, :, None
    ]
    out = jnp.where(trailing, update, 0.0)

    qc = jnp.minimum(q, PANELS - 1)
    pc = jnp.minimum(p, PANELS - 1)
    panel_vals = lax.dynamic_slice_in_dim(rows_solved, qc * tile, tile, axis=2)
    diag_tile = lax.dynamic_slice(factor, (pc * tile, qc * tile), (tile, tile))
    panel_vals = panel_vals.at[0].set(jnp.where(p < PANELS, diag_tile, panel_vals[0]))
    out = out.at[:, :, 0, :].set(jnp.where(q < PANELS, panel_vals, out[:, :, 0, :]))
    return out.reshape(1, rt, tile, 1, ct, tile)


def solution(mesh):
    return jax.shard_map(
        per_device,
        mesh=mesh,
        in_specs=(P("prow", None, None, "pcol", None, None),),
        out_specs=P("prow", None, None, "pcol", None, None),
        check_vma=False,
    )
```

```python
import jax
import jax.numpy as jnp
from jax import lax
from jax.sharding import PartitionSpec as P

PANELS = 2
HI = lax.Precision.HIGHEST


def prow_from_first_two(x, prows):
    me = lax.axis_index("prow")
    got = [x]
    for d in range(1, prows):
        got.append(lax.ppermute(x, "prow", [(0, d), (1, (1 + d) % prows)]))
    stack = jnp.stack(got)
    return stack[me], stack[(me + prows - 1) % prows]


def diag_to_first_pcols(tile0, prows, pcols):
    me = lax.axis_index("prow")
    got = [tile0]
    for d in range(1, prows):
        pairs = []
        for q in range(PANELS):
            pairs.append((q, d * pcols + q))
            pairs.append((pcols + q, ((1 + d) % prows) * pcols + q))
        got.append(lax.ppermute(tile0, ("prow", "pcol"), pairs))
    stack = jnp.stack(got)
    return stack[me], stack[(me + prows - 1) % prows]


def pcol_tree_rounds(pcols):
    zs = pcols // 4

    def idx(x, z, core):
        return (x * zs + z % zs) * 2 + core

    rounds = []
    a_have = [(0, 0)]
    b_have = [(0, 0)]
    steps_a = [("x", 0), ("z", zs // 2)]
    steps_b = [("z", zs // 2), ("x", 0)]
    s = zs // 4
    while s >= 1:
        steps_a.append(("z", s))
        steps_b.append(("z", -s))
        s //= 2
    for (ka, da), (kb, db) in zip(steps_a, steps_b):
        pairs = []
        new_a = []
        for x, z in a_have:
            t = (1 - x, z) if ka == "x" else (x, (z + da) % zs)
            pairs.append((idx(x, z, 0), idx(t[0], t[1], 0)))
            new_a.append(t)
        new_b = []
        for x, z in b_have:
            t = (1 - x, z) if kb == "x" else (x, (z + db) % zs)
            pairs.append((idx(x, z, 1), idx(t[0], t[1], 1)))
            new_b.append(t)
        a_have += new_a
        b_have += new_b
        rounds.append(pairs)
    return rounds


def pcol_broadcast_pair(buf, pcols):
    me = lax.axis_index("pcol")
    for pairs in pcol_tree_rounds(pcols):
        got = lax.ppermute(buf, "pcol", pairs)
        targets = jnp.array([t for _, t in pairs], jnp.int32)
        hit = jnp.any(targets == me)
        buf = jnp.where(hit, got, buf)
    other = lax.ppermute(buf, "pcol", [(i, i ^ 1) for i in range(pcols)])
    core0 = (me % 2) == 0
    return jnp.where(core0, buf, other), jnp.where(core0, other, buf)


def per_device(covariance):
    prows = lax.axis_size("prow")
    pcols = lax.axis_size("pcol")
    p = lax.axis_index("prow")
    q = lax.axis_index("pcol")
    rt = covariance.shape[1]
    tile = covariance.shape[2]
    ct = covariance.shape[4]
    nb = PANELS * tile
    tiles = covariance.reshape(rt, tile, ct, tile)

    first, second = diag_to_first_pcols(tiles[0, :, 0, :], prows, pcols)
    diag_a, diag_b = pcol_broadcast_pair(jnp.stack([first, second]), pcols)
    block = jnp.concatenate(
        [
            jnp.concatenate([diag_a[0], diag_b[0]], axis=1),
            jnp.concatenate([diag_a[1], diag_b[1]], axis=1),
        ],
        axis=0,
    )

    cols_src = lax.optimization_barrier((tiles[0], first, second))[0]
    t0, t1 = prow_from_first_two(cols_src, prows)

    rows_src = lax.optimization_barrier((tiles[:, :, 0, :], diag_a, diag_b))[0]
    col0, col1 = pcol_broadcast_pair(rows_src, pcols)

    factor = jnp.tril(jnp.linalg.cholesky(block))
    inverse = jax.scipy.linalg.solve_triangular(
        factor, jnp.eye(nb, dtype=factor.dtype), lower=True
    )

    rows_panel = jnp.concatenate([col0, col1], axis=-1)
    cols_panel = jnp.concatenate(
        [jnp.transpose(t0, (1, 2, 0)), jnp.transpose(t1, (1, 2, 0))], axis=-1
    )
    rows_solved = jnp.einsum("rak,bk->rab", rows_panel, inverse, precision=HI)
    cols_solved = jnp.einsum("cak,bk->cab", cols_panel, inverse, precision=HI)
    update = tiles - jnp.einsum("rak,cbk->racb", rows_solved, cols_solved, precision=HI)

    row_index = jnp.arange(rt, dtype=jnp.int32) * prows + p
    col_index = jnp.arange(ct, dtype=jnp.int32) * pcols + q
    trailing = (row_index >= PANELS)[:, None, None, None] & (col_index >= PANELS)[
        None, None, :, None
    ]
    out = jnp.where(trailing, update, 0.0)

    qc = jnp.minimum(q, PANELS - 1)
    pc = jnp.minimum(p, PANELS - 1)
    panel_vals = lax.dynamic_slice_in_dim(rows_solved, qc * tile, tile, axis=2)
    diag_tile = lax.dynamic_slice(factor, (pc * tile, qc * tile), (tile, tile))
    panel_vals = panel_vals.at[0].set(jnp.where(p < PANELS, diag_tile, panel_vals[0]))
    out = out.at[:, :, 0, :].set(jnp.where(q < PANELS, panel_vals, out[:, :, 0, :]))
    return out.reshape(1, rt, tile, 1, ct, tile)


def solution(mesh):
    return jax.shard_map(
        per_device,
        mesh=mesh,
        in_specs=(P("prow", None, None, "pcol", None, None),),
        out_specs=P("prow", None, None, "pcol", None, None),
        check_vma=False,
    )
```

```python
import jax
import jax.numpy as jnp
from jax import lax
from jax.sharding import PartitionSpec as P

PANELS = 2
HI = lax.Precision.HIGHEST


def prow_from_first_two(x, prows):
    me = lax.axis_index("prow")
    got = [x]
    for d in range(1, prows):
        got.append(lax.ppermute(x, "prow", [(0, d), (1, (1 + d) % prows)]))
    stack = jnp.stack(got)
    return stack[me], stack[(me + prows - 1) % prows]


def diag_to_first_pcols(tile0, prows, pcols):
    me = lax.axis_index("prow")
    got = [tile0]
    for d in range(1, prows):
        pairs = []
        for q in range(PANELS):
            pairs.append((q, d * pcols + q))
            pairs.append((pcols + q, ((1 + d) % prows) * pcols + q))
        got.append(lax.ppermute(tile0, ("prow", "pcol"), pairs))
    stack = jnp.stack(got)
    return stack[me], stack[(me + prows - 1) % prows]


def pcol_tree_rounds(pcols):
    zs = pcols // 4

    def idx(x, z, core):
        return (x * zs + z % zs) * 2 + core

    rounds = []
    a_have = [(0, 0)]
    b_have = [(0, 0)]
    steps_a = [("x", 0), ("z", zs // 2)]
    steps_b = [("z", zs // 2), ("x", 0)]
    s = zs // 4
    while s >= 1:
        steps_a.append(("z", s))
        steps_b.append(("z", -s))
        s //= 2
    for (ka, da), (kb, db) in zip(steps_a, steps_b):
        pairs = []
        new_a = []
        for x, z in a_have:
            t = (1 - x, z) if ka == "x" else (x, (z + da) % zs)
            pairs.append((idx(x, z, 0), idx(t[0], t[1], 0)))
            new_a.append(t)
        new_b = []
        for x, z in b_have:
            t = (1 - x, z) if kb == "x" else (x, (z + db) % zs)
            pairs.append((idx(x, z, 1), idx(t[0], t[1], 1)))
            new_b.append(t)
        a_have += new_a
        b_have += new_b
        rounds.append(pairs)
    return rounds


def pcol_broadcast_pair(buf, pcols):
    me = lax.axis_index("pcol")
    for pairs in pcol_tree_rounds(pcols):
        got = lax.ppermute(buf, "pcol", pairs)
        targets = jnp.array([t for _, t in pairs], jnp.int32)
        hit = jnp.any(targets == me)
        buf = jnp.where(hit, got, buf)
    other = lax.ppermute(buf, "pcol", [(i, i ^ 1) for i in range(pcols)])
    core0 = (me % 2) == 0
    return jnp.where(core0, buf, other), jnp.where(core0, other, buf)


def per_device(covariance):
    prows = lax.axis_size("prow")
    pcols = lax.axis_size("pcol")
    p = lax.axis_index("prow")
    q = lax.axis_index("pcol")
    rt = covariance.shape[1]
    tile = covariance.shape[2]
    ct = covariance.shape[4]
    nb = PANELS * tile
    tiles = covariance.reshape(rt, tile, ct, tile)

    first, second = diag_to_first_pcols(tiles[0, :, 0, :], prows, pcols)
    diag_a, diag_b = pcol_broadcast_pair(jnp.stack([first, second]), pcols)
    block = jnp.concatenate(
        [
            jnp.concatenate([diag_a[0], diag_b[0]], axis=1),
            jnp.concatenate([diag_a[1], diag_b[1]], axis=1),
        ],
        axis=0,
    )

    rows_src = lax.optimization_barrier((tiles[:, :, 0, :], diag_a, diag_b))[0]
    col0, col1 = pcol_broadcast_pair(rows_src, pcols)

    factor = jnp.tril(jnp.linalg.cholesky(block))

    cols_src = lax.optimization_barrier((tiles[0], factor))[0]
    t0, t1 = prow_from_first_two(cols_src, prows)

    inverse = jax.scipy.linalg.solve_triangular(
        factor, jnp.eye(nb, dtype=factor.dtype), lower=True
    )

    rows_panel = jnp.concatenate([col0, col1], axis=-1)
    cols_panel = jnp.concatenate(
        [jnp.transpose(t0, (1, 2, 0)), jnp.transpose(t1, (1, 2, 0))], axis=-1
    )
    rows_solved = jnp.einsum("rak,bk->rab", rows_panel, inverse, precision=HI)
    cols_solved = jnp.einsum("cak,bk->cab", cols_panel, inverse, precision=HI)
    update = tiles - jnp.einsum("rak,cbk->racb", rows_solved, cols_solved, precision=HI)

    row_index = jnp.arange(rt, dtype=jnp.int32) * prows + p
    col_index = jnp.arange(ct, dtype=jnp.int32) * pcols + q
    trailing = (row_index >= PANELS)[:, None, None, None] & (col_index >= PANELS)[
        None, None, :, None
    ]
    out = jnp.where(trailing, update, 0.0)

    qc = jnp.minimum(q, PANELS - 1)
    pc = jnp.minimum(p, PANELS - 1)
    panel_vals = lax.dynamic_slice_in_dim(rows_solved, qc * tile, tile, axis=2)
    diag_tile = lax.dynamic_slice(factor, (pc * tile, qc * tile), (tile, tile))
    panel_vals = panel_vals.at[0].set(jnp.where(p < PANELS, diag_tile, panel_vals[0]))
    out = out.at[:, :, 0, :].set(jnp.where(q < PANELS, panel_vals, out[:, :, 0, :]))
    return out.reshape(1, rt, tile, 1, ct, tile)


def solution(mesh):
    return jax.shard_map(
        per_device,
        mesh=mesh,
        in_specs=(P("prow", None, None, "pcol", None, None),),
        out_specs=P("prow", None, None, "pcol", None, None),
        check_vma=False,
    )
```

```python
import jax
import jax.numpy as jnp
from jax import lax
from jax.sharding import PartitionSpec as P

PANELS = 2
HI = lax.Precision.HIGHEST


def prow_from_first_two(x, prows):
    me = lax.axis_index("prow")
    other = lax.ppermute(x, "prow", [(0, 1), (1, 0)])
    pair = jnp.where(me == 0, jnp.stack([x, other]), jnp.stack([other, x]))
    have = 2
    while have < prows:
        step = prows // 2 if have == 2 else have // 2
        span = 2 * step
        pairs = [(i, i + step) for i in range(prows) if i % span < 2 and i + step < prows]
        got = lax.ppermute(pair, "prow", pairs)
        targets = jnp.array([t for _, t in pairs], jnp.int32)
        pair = jnp.where(jnp.any(targets == me), got, pair)
        have *= 2
    return pair[0], pair[1]


def diag_to_first_pcols(tile0, prows, pcols):
    me = lax.axis_index("prow")
    got = [tile0]
    for d in range(1, prows):
        pairs = []
        for q in range(PANELS):
            pairs.append((q, d * pcols + q))
            pairs.append((pcols + q, ((1 + d) % prows) * pcols + q))
        got.append(lax.ppermute(tile0, ("prow", "pcol"), pairs))
    stack = jnp.stack(got)
    return stack[me], stack[(me + prows - 1) % prows]


def pcol_tree_rounds(pcols):
    zs = pcols // 4

    def idx(x, z, core):
        return (x * zs + z % zs) * 2 + core

    rounds = []
    a_have = [(0, 0)]
    b_have = [(0, 0)]
    steps_a = [("x", 0), ("z", zs // 2)]
    steps_b = [("z", zs // 2), ("x", 0)]
    s = zs // 4
    while s >= 1:
        steps_a.append(("z", s))
        steps_b.append(("z", -s))
        s //= 2
    for (ka, da), (kb, db) in zip(steps_a, steps_b):
        pairs = []
        new_a = []
        for x, z in a_have:
            t = (1 - x, z) if ka == "x" else (x, (z + da) % zs)
            pairs.append((idx(x, z, 0), idx(t[0], t[1], 0)))
            new_a.append(t)
        new_b = []
        for x, z in b_have:
            t = (1 - x, z) if kb == "x" else (x, (z + db) % zs)
            pairs.append((idx(x, z, 1), idx(t[0], t[1], 1)))
            new_b.append(t)
        a_have += new_a
        b_have += new_b
        rounds.append(pairs)
    return rounds


def pcol_broadcast_pair(buf, pcols):
    me = lax.axis_index("pcol")
    for pairs in pcol_tree_rounds(pcols):
        got = lax.ppermute(buf, "pcol", pairs)
        targets = jnp.array([t for _, t in pairs], jnp.int32)
        hit = jnp.any(targets == me)
        buf = jnp.where(hit, got, buf)
    other = lax.ppermute(buf, "pcol", [(i, i ^ 1) for i in range(pcols)])
    core0 = (me % 2) == 0
    return jnp.where(core0, buf, other), jnp.where(core0, other, buf)


def per_device(covariance):
    prows = lax.axis_size("prow")
    pcols = lax.axis_size("pcol")
    p = lax.axis_index("prow")
    q = lax.axis_index("pcol")
    rt = covariance.shape[1]
    tile = covariance.shape[2]
    ct = covariance.shape[4]
    tiles = covariance.reshape(rt, tile, ct, tile)

    first, second = diag_to_first_pcols(tiles[0, :, 0, :], prows, pcols)
    diag_a, diag_b = pcol_broadcast_pair(jnp.stack([first, second]), pcols)

    rows_src = lax.optimization_barrier((tiles[:, :, 0, :], diag_a, diag_b))[0]
    col0, col1 = pcol_broadcast_pair(rows_src, pcols)

    a00, a10 = diag_a[0], diag_a[1]
    a11 = diag_b[1]
    eye = jnp.eye(tile, dtype=a00.dtype)
    l00 = jnp.tril(jnp.linalg.cholesky(a00))

    cols_src = lax.optimization_barrier((tiles[0], l00))[0]
    t0, t1 = prow_from_first_two(cols_src, prows)

    l00_inv = jax.scipy.linalg.solve_triangular(l00, eye, lower=True)
    l10 = jnp.dot(a10, l00_inv.T, precision=HI)
    schur = a11 - jnp.dot(l10, l10.T, precision=HI)
    l11 = jnp.tril(jnp.linalg.cholesky(schur))
    l11_inv = jax.scipy.linalg.solve_triangular(l11, eye, lower=True)
    low_inv = -jnp.dot(l11_inv, jnp.dot(l10, l00_inv, precision=HI), precision=HI)
    zero = jnp.zeros_like(eye)
    factor = jnp.concatenate(
        [jnp.concatenate([l00, zero], axis=1), jnp.concatenate([l10, l11], axis=1)], axis=0
    )
    inverse = jnp.concatenate(
        [jnp.concatenate([l00_inv, zero], axis=1), jnp.concatenate([low_inv, l11_inv], axis=1)],
        axis=0,
    )

    rows_panel = jnp.concatenate([col0, col1], axis=-1)
    cols_panel = jnp.concatenate(
        [jnp.transpose(t0, (1, 2, 0)), jnp.transpose(t1, (1, 2, 0))], axis=-1
    )
    rows_solved = jnp.einsum("rak,bk->rab", rows_panel, inverse, precision=HI)
    cols_solved = jnp.einsum("cak,bk->cab", cols_panel, inverse, precision=HI)
    update = tiles - jnp.einsum("rak,cbk->racb", rows_solved, cols_solved, precision=HI)

    row_index = jnp.arange(rt, dtype=jnp.int32) * prows + p
    col_index = jnp.arange(ct, dtype=jnp.int32) * pcols + q
    trailing = (row_index >= PANELS)[:, None, None, None] & (col_index >= PANELS)[
        None, None, :, None
    ]
    out = jnp.where(trailing, update, 0.0)

    qc = jnp.minimum(q, PANELS - 1)
    pc = jnp.minimum(p, PANELS - 1)
    panel_vals = lax.dynamic_slice_in_dim(rows_solved, qc * tile, tile, axis=2)
    diag_tile = lax.dynamic_slice(factor, (pc * tile, qc * tile), (tile, tile))
    panel_vals = panel_vals.at[0].set(jnp.where(p < PANELS, diag_tile, panel_vals[0]))
    out = out.at[:, :, 0, :].set(jnp.where(q < PANELS, panel_vals, out[:, :, 0, :]))
    return out.reshape(1, rt, tile, 1, ct, tile)


def solution(mesh):
    return jax.shard_map(
        per_device,
        mesh=mesh,
        in_specs=(P("prow", None, None, "pcol", None, None),),
        out_specs=P("prow", None, None, "pcol", None, None),
        check_vma=False,
    )
```

```python
import jax
import jax.numpy as jnp
from jax import lax
from jax.sharding import PartitionSpec as P

PANELS = 2
HI = lax.Precision.HIGHEST


def prow_from_first_two(x, prows):
    me = lax.axis_index("prow")
    other = lax.ppermute(x, "prow", [(0, 1), (1, 0)])
    pair = jnp.where(me == 0, jnp.stack([x, other]), jnp.stack([other, x]))
    have = 2
    while have < prows:
        step = prows // 2 if have == 2 else have // 2
        span = 2 * step
        pairs = [(i, i + step) for i in range(prows) if i % span < 2 and i + step < prows]
        got = lax.ppermute(pair, "prow", pairs)
        targets = jnp.array([t for _, t in pairs], jnp.int32)
        pair = jnp.where(jnp.any(targets == me), got, pair)
        have *= 2
    return pair[0], pair[1]


def diag_to_first_pcols(tile0, prows, pcols):
    me = lax.axis_index("prow")
    got = [tile0]
    for d in range(1, prows):
        pairs = []
        for q in range(PANELS):
            pairs.append((q, d * pcols + q))
            pairs.append((pcols + q, ((1 + d) % prows) * pcols + q))
        got.append(lax.ppermute(tile0, ("prow", "pcol"), pairs))
    stack = jnp.stack(got)
    return stack[me], stack[(me + prows - 1) % prows]


def pcol_tree_rounds(pcols):
    zs = pcols // 4

    def idx(x, z, core):
        return (x * zs + z % zs) * 2 + core

    rounds = []
    a_have = [(0, 0)]
    b_have = [(0, 0)]
    steps_a = [("x", 0), ("z", zs // 2)]
    steps_b = [("z", zs // 2), ("x", 0)]
    s = zs // 4
    while s >= 1:
        steps_a.append(("z", s))
        steps_b.append(("z", -s))
        s //= 2
    for (ka, da), (kb, db) in zip(steps_a, steps_b):
        pairs = []
        new_a = []
        for x, z in a_have:
            t = (1 - x, z) if ka == "x" else (x, (z + da) % zs)
            pairs.append((idx(x, z, 0), idx(t[0], t[1], 0)))
            new_a.append(t)
        new_b = []
        for x, z in b_have:
            t = (1 - x, z) if kb == "x" else (x, (z + db) % zs)
            pairs.append((idx(x, z, 1), idx(t[0], t[1], 1)))
            new_b.append(t)
        a_have += new_a
        b_have += new_b
        rounds.append(pairs)
    return rounds


def pcol_broadcast_pair(buf, pcols):
    me = lax.axis_index("pcol")
    for pairs in pcol_tree_rounds(pcols):
        got = lax.ppermute(buf, "pcol", pairs)
        targets = jnp.array([t for _, t in pairs], jnp.int32)
        hit = jnp.any(targets == me)
        buf = jnp.where(hit, got, buf)
    other = lax.ppermute(buf, "pcol", [(i, i ^ 1) for i in range(pcols)])
    core0 = (me % 2) == 0
    return jnp.where(core0, buf, other), jnp.where(core0, other, buf)


def per_device(covariance):
    prows = lax.axis_size("prow")
    pcols = lax.axis_size("pcol")
    p = lax.axis_index("prow")
    q = lax.axis_index("pcol")
    rt = covariance.shape[1]
    tile = covariance.shape[2]
    ct = covariance.shape[4]
    tiles = covariance.reshape(rt, tile, ct, tile)

    first, second = diag_to_first_pcols(tiles[0, :, 0, :], prows, pcols)
    diag_a, diag_b = pcol_broadcast_pair(jnp.stack([first, second]), pcols)

    cols_src = lax.optimization_barrier((tiles[0], first, second))[0]
    t0, t1 = prow_from_first_two(cols_src, prows)

    a00, a10 = diag_a[0], diag_a[1]
    a11 = diag_b[1]
    eye = jnp.eye(tile, dtype=a00.dtype)
    l00 = jnp.tril(jnp.linalg.cholesky(a00))

    rows_src = lax.optimization_barrier((tiles[:, :, 0, :], l00))[0]
    col0, col1 = pcol_broadcast_pair(rows_src, pcols)

    l00_inv = jax.scipy.linalg.solve_triangular(l00, eye, lower=True)
    l10 = jnp.dot(a10, l00_inv.T, precision=HI)
    schur = a11 - jnp.dot(l10, l10.T, precision=HI)
    l11 = jnp.tril(jnp.linalg.cholesky(schur))
    l11_inv = jax.scipy.linalg.solve_triangular(l11, eye, lower=True)
    low_inv = -jnp.dot(l11_inv, jnp.dot(l10, l00_inv, precision=HI), precision=HI)
    zero = jnp.zeros_like(eye)
    factor = jnp.concatenate(
        [jnp.concatenate([l00, zero], axis=1), jnp.concatenate([l10, l11], axis=1)], axis=0
    )
    inverse = jnp.concatenate(
        [jnp.concatenate([l00_inv, zero], axis=1), jnp.concatenate([low_inv, l11_inv], axis=1)],
        axis=0,
    )

    rows_panel = jnp.concatenate([col0, col1], axis=-1)
    cols_panel = jnp.concatenate(
        [jnp.transpose(t0, (1, 2, 0)), jnp.transpose(t1, (1, 2, 0))], axis=-1
    )
    rows_solved = jnp.einsum("rak,bk->rab", rows_panel, inverse, precision=HI)
    cols_solved = jnp.einsum("cak,bk->cab", cols_panel, inverse, precision=HI)
    update = tiles - jnp.einsum("rak,cbk->racb", rows_solved, cols_solved, precision=HI)

    row_index = jnp.arange(rt, dtype=jnp.int32) * prows + p
    col_index = jnp.arange(ct, dtype=jnp.int32) * pcols + q
    trailing = (row_index >= PANELS)[:, None, None, None] & (col_index >= PANELS)[
        None, None, :, None
    ]
    out = jnp.where(trailing, update, 0.0)

    qc = jnp.minimum(q, PANELS - 1)
    pc = jnp.minimum(p, PANELS - 1)
    panel_vals = lax.dynamic_slice_in_dim(rows_solved, qc * tile, tile, axis=2)
    diag_tile = lax.dynamic_slice(factor, (pc * tile, qc * tile), (tile, tile))
    panel_vals = panel_vals.at[0].set(jnp.where(p < PANELS, diag_tile, panel_vals[0]))
    out = out.at[:, :, 0, :].set(jnp.where(q < PANELS, panel_vals, out[:, :, 0, :]))
    return out.reshape(1, rt, tile, 1, ct, tile)


def solution(mesh):
    return jax.shard_map(
        per_device,
        mesh=mesh,
        in_specs=(P("prow", None, None, "pcol", None, None),),
        out_specs=P("prow", None, None, "pcol", None, None),
        check_vma=False,
    )
```

```python
import jax
import jax.numpy as jnp
from jax import lax
from jax.sharding import PartitionSpec as P

PANELS = 2
HI = lax.Precision.HIGHEST


def prow_from_first_two(x, prows):
    me = lax.axis_index("prow")
    other = lax.ppermute(x, "prow", [(0, 1), (1, 0)])
    pair = jnp.where(me == 0, jnp.stack([x, other]), jnp.stack([other, x]))
    have = 2
    while have < prows:
        step = prows // 2 if have == 2 else have // 2
        span = 2 * step
        pairs = [(i, i + step) for i in range(prows) if i % span < 2 and i + step < prows]
        got = lax.ppermute(pair, "prow", pairs)
        targets = jnp.array([t for _, t in pairs], jnp.int32)
        pair = jnp.where(jnp.any(targets == me), got, pair)
        have *= 2
    return pair[0], pair[1]


def diag_to_first_pcols(tile0, prows, pcols):
    me = lax.axis_index("prow")
    got = [tile0]
    for d in range(1, prows):
        pairs = []
        for q in range(PANELS):
            pairs.append((q, d * pcols + q))
            pairs.append((pcols + q, ((1 + d) % prows) * pcols + q))
        got.append(lax.ppermute(tile0, ("prow", "pcol"), pairs))
    stack = jnp.stack(got)
    return stack[me], stack[(me + prows - 1) % prows]


def pcol_tree_rounds(pcols):
    zs = pcols // 4

    def idx(x, z, core):
        return (x * zs + z % zs) * 2 + core

    rounds = []
    a_have = [(0, 0)]
    b_have = [(0, 0)]
    steps_a = [("x", 0), ("z", zs // 2)]
    steps_b = [("z", zs // 2), ("x", 0)]
    s = zs // 4
    while s >= 1:
        steps_a.append(("z", s))
        steps_b.append(("z", -s))
        s //= 2
    for (ka, da), (kb, db) in zip(steps_a, steps_b):
        pairs = []
        new_a = []
        for x, z in a_have:
            t = (1 - x, z) if ka == "x" else (x, (z + da) % zs)
            pairs.append((idx(x, z, 0), idx(t[0], t[1], 0)))
            new_a.append(t)
        new_b = []
        for x, z in b_have:
            t = (1 - x, z) if kb == "x" else (x, (z + db) % zs)
            pairs.append((idx(x, z, 1), idx(t[0], t[1], 1)))
            new_b.append(t)
        a_have += new_a
        b_have += new_b
        rounds.append(pairs)
    return rounds


def pcol_broadcast_pair(buf, pcols):
    me = lax.axis_index("pcol")
    for pairs in pcol_tree_rounds(pcols):
        got = lax.ppermute(buf, "pcol", pairs)
        targets = jnp.array([t for _, t in pairs], jnp.int32)
        hit = jnp.any(targets == me)
        buf = jnp.where(hit, got, buf)
    other = lax.ppermute(buf, "pcol", [(i, i ^ 1) for i in range(pcols)])
    core0 = (me % 2) == 0
    return jnp.where(core0, buf, other), jnp.where(core0, other, buf)


def per_device(covariance):
    prows = lax.axis_size("prow")
    pcols = lax.axis_size("pcol")
    p = lax.axis_index("prow")
    q = lax.axis_index("pcol")
    rt = covariance.shape[1]
    tile = covariance.shape[2]
    ct = covariance.shape[4]
    tiles = covariance.reshape(rt, tile, ct, tile)

    first, second = diag_to_first_pcols(tiles[0, :, 0, :], prows, pcols)
    diag_a, diag_b = pcol_broadcast_pair(jnp.stack([first, second]), pcols)

    t0, t1 = prow_from_first_two(tiles[0], prows)

    a00, a10 = diag_a[0], diag_a[1]
    a11 = diag_b[1]
    eye = jnp.eye(tile, dtype=a00.dtype)
    l00 = jnp.tril(jnp.linalg.cholesky(a00))

    col0, col1 = pcol_broadcast_pair(tiles[:, :, 0, :], pcols)

    l00_inv = jax.scipy.linalg.solve_triangular(l00, eye, lower=True)
    l10 = jnp.dot(a10, l00_inv.T, precision=HI)
    schur = a11 - jnp.dot(l10, l10.T, precision=HI)
    l11 = jnp.tril(jnp.linalg.cholesky(schur))
    l11_inv = jax.scipy.linalg.solve_triangular(l11, eye, lower=True)
    low_inv = -jnp.dot(l11_inv, jnp.dot(l10, l00_inv, precision=HI), precision=HI)
    zero = jnp.zeros_like(eye)
    factor = jnp.concatenate(
        [jnp.concatenate([l00, zero], axis=1), jnp.concatenate([l10, l11], axis=1)], axis=0
    )
    inverse = jnp.concatenate(
        [jnp.concatenate([l00_inv, zero], axis=1), jnp.concatenate([low_inv, l11_inv], axis=1)],
        axis=0,
    )

    rows_panel = jnp.concatenate([col0, col1], axis=-1)
    cols_panel = jnp.concatenate(
        [jnp.transpose(t0, (1, 2, 0)), jnp.transpose(t1, (1, 2, 0))], axis=-1
    )
    rows_solved = jnp.einsum("rak,bk->rab", rows_panel, inverse, precision=HI)
    cols_solved = jnp.einsum("cak,bk->cab", cols_panel, inverse, precision=HI)
    update = tiles - jnp.einsum("rak,cbk->racb", rows_solved, cols_solved, precision=HI)

    row_index = jnp.arange(rt, dtype=jnp.int32) * prows + p
    col_index = jnp.arange(ct, dtype=jnp.int32) * pcols + q
    trailing = (row_index >= PANELS)[:, None, None, None] & (col_index >= PANELS)[
        None, None, :, None
    ]
    out = jnp.where(trailing, update, 0.0)

    qc = jnp.minimum(q, PANELS - 1)
    pc = jnp.minimum(p, PANELS - 1)
    panel_vals = lax.dynamic_slice_in_dim(rows_solved, qc * tile, tile, axis=2)
    diag_tile = lax.dynamic_slice(factor, (pc * tile, qc * tile), (tile, tile))
    panel_vals = panel_vals.at[0].set(jnp.where(p < PANELS, diag_tile, panel_vals[0]))
    out = out.at[:, :, 0, :].set(jnp.where(q < PANELS, panel_vals, out[:, :, 0, :]))
    return out.reshape(1, rt, tile, 1, ct, tile)


def solution(mesh):
    return jax.shard_map(
        per_device,
        mesh=mesh,
        in_specs=(P("prow", None, None, "pcol", None, None),),
        out_specs=P("prow", None, None, "pcol", None, None),
        check_vma=False,
    )
```

```python
import jax
import jax.numpy as jnp
from jax import lax
from jax.sharding import PartitionSpec as P

PANELS = 2
HI = lax.Precision.HIGHEST


def prow_from_first_two(x, prows):
    me = lax.axis_index("prow")
    other = lax.ppermute(x, "prow", [(0, 1), (1, 0)])
    pair = jnp.where(me == 0, jnp.stack([x, other]), jnp.stack([other, x]))
    have = 2
    while have < prows:
        step = prows // 2 if have == 2 else have // 2
        span = 2 * step
        pairs = [(i, i + step) for i in range(prows) if i % span < 2 and i + step < prows]
        got = lax.ppermute(pair, "prow", pairs)
        targets = jnp.array([t for _, t in pairs], jnp.int32)
        pair = jnp.where(jnp.any(targets == me), got, pair)
        have *= 2
    return pair[0], pair[1]


def diag_to_first_pcols(tile0, prows, pcols):
    me = lax.axis_index("prow")
    got = [tile0]
    for d in range(1, prows):
        pairs = []
        for q in range(PANELS):
            pairs.append((q, d * pcols + q))
            pairs.append((pcols + q, ((1 + d) % prows) * pcols + q))
        got.append(lax.ppermute(tile0, ("prow", "pcol"), pairs))
    stack = jnp.stack(got)
    return stack[me], stack[(me + prows - 1) % prows]


def pcol_tree_rounds(pcols):
    zs = pcols // 4

    def idx(x, z, core):
        return (x * zs + z % zs) * 2 + core

    rounds = []
    a_have = [(0, 0)]
    b_have = [(0, 0)]
    steps_a = [("x", 0), ("z", zs // 2)]
    steps_b = [("z", zs // 2), ("x", 0)]
    s = zs // 4
    while s >= 1:
        steps_a.append(("z", s))
        steps_b.append(("z", -s))
        s //= 2
    for (ka, da), (kb, db) in zip(steps_a, steps_b):
        pairs = []
        new_a = []
        for x, z in a_have:
            t = (1 - x, z) if ka == "x" else (x, (z + da) % zs)
            pairs.append((idx(x, z, 0), idx(t[0], t[1], 0)))
            new_a.append(t)
        new_b = []
        for x, z in b_have:
            t = (1 - x, z) if kb == "x" else (x, (z + db) % zs)
            pairs.append((idx(x, z, 1), idx(t[0], t[1], 1)))
            new_b.append(t)
        a_have += new_a
        b_have += new_b
        rounds.append(pairs)
    return rounds


def pcol_broadcast_pair(buf, pcols):
    me = lax.axis_index("pcol")
    for pairs in pcol_tree_rounds(pcols):
        got = lax.ppermute(buf, "pcol", pairs)
        targets = jnp.array([t for _, t in pairs], jnp.int32)
        hit = jnp.any(targets == me)
        buf = jnp.where(hit, got, buf)
    other = lax.ppermute(buf, "pcol", [(i, i ^ 1) for i in range(pcols)])
    core0 = (me % 2) == 0
    return jnp.where(core0, buf, other), jnp.where(core0, other, buf)


def per_device(covariance):
    prows = lax.axis_size("prow")
    pcols = lax.axis_size("pcol")
    p = lax.axis_index("prow")
    q = lax.axis_index("pcol")
    rt = covariance.shape[1]
    tile = covariance.shape[2]
    ct = covariance.shape[4]
    tiles = covariance.reshape(rt, tile, ct, tile)

    first, second = diag_to_first_pcols(tiles[0, :, 0, :], prows, pcols)
    diag_a, diag_b = pcol_broadcast_pair(jnp.stack([first, second]), pcols)

    t0, t1 = prow_from_first_two(tiles[0], prows)

    a00, a10 = diag_a[0], diag_a[1]
    a11 = diag_b[1]
    eye = jnp.eye(tile, dtype=a00.dtype)
    l00 = jnp.tril(jnp.linalg.cholesky(a00))

    col0, col1 = pcol_broadcast_pair(tiles[:, :, 0, :], pcols)

    l00_inv = jax.scipy.linalg.solve_triangular(l00, eye, lower=True)
    l10 = jnp.dot(a10, l00_inv.T, precision=HI)
    schur = a11 - jnp.dot(l10, l10.T, precision=HI)
    l11 = jnp.tril(jnp.linalg.cholesky(schur))
    l11_inv = jax.scipy.linalg.solve_triangular(l11, eye, lower=True)
    low_inv = -jnp.dot(l11_inv, jnp.dot(l10, l00_inv, precision=HI), precision=HI)
    zero = jnp.zeros_like(eye)
    factor = jnp.concatenate(
        [jnp.concatenate([l00, zero], axis=1), jnp.concatenate([l10, l11], axis=1)], axis=0
    )
    inverse = jnp.concatenate(
        [jnp.concatenate([l00_inv, zero], axis=1), jnp.concatenate([low_inv, l11_inv], axis=1)],
        axis=0,
    )

    rows_panel = jnp.concatenate([col0, col1], axis=-1)
    cols_panel = jnp.concatenate(
        [jnp.transpose(t0, (1, 2, 0)), jnp.transpose(t1, (1, 2, 0))], axis=-1
    )
    cols_solved = jnp.einsum("cak,bk->cab", cols_panel, inverse, precision=HI)
    folded = jnp.einsum("mk,cbm->ckb", inverse, cols_solved, precision=HI)
    update = tiles - jnp.einsum("rak,ckb->racb", rows_panel, folded, precision=HI)

    row_index = jnp.arange(rt, dtype=jnp.int32) * prows + p
    col_index = jnp.arange(ct, dtype=jnp.int32) * pcols + q
    trailing = (row_index >= PANELS)[:, None, None, None] & (col_index >= PANELS)[
        None, None, :, None
    ]
    out = jnp.where(trailing, update, 0.0)

    qc = jnp.minimum(q, PANELS - 1)
    pc = jnp.minimum(p, PANELS - 1)
    inverse_rows = lax.dynamic_slice_in_dim(inverse, qc * tile, tile, axis=0)
    panel_vals = jnp.einsum("rak,bk->rab", rows_panel, inverse_rows, precision=HI)
    diag_tile = lax.dynamic_slice(factor, (pc * tile, qc * tile), (tile, tile))
    panel_vals = panel_vals.at[0].set(jnp.where(p < PANELS, diag_tile, panel_vals[0]))
    out = out.at[:, :, 0, :].set(jnp.where(q < PANELS, panel_vals, out[:, :, 0, :]))
    return out.reshape(1, rt, tile, 1, ct, tile)


def solution(mesh):
    return jax.shard_map(
        per_device,
        mesh=mesh,
        in_specs=(P("prow", None, None, "pcol", None, None),),
        out_specs=P("prow", None, None, "pcol", None, None),
        check_vma=False,
    )
```

```python
import jax
import jax.numpy as jnp
from jax import lax
from jax.sharding import PartitionSpec as P

PANELS = 2
HI = lax.Precision.HIGHEST


def prow_from_first_two(x, prows):
    me = lax.axis_index("prow")
    other = lax.ppermute(x, "prow", [(0, 1), (1, 0)])
    pair = jnp.where(me == 0, jnp.stack([x, other]), jnp.stack([other, x]))
    have = 2
    while have < prows:
        step = prows // 2 if have == 2 else have // 2
        span = 2 * step
        pairs = [(i, i + step) for i in range(prows) if i % span < 2 and i + step < prows]
        got = lax.ppermute(pair, "prow", pairs)
        targets = jnp.array([t for _, t in pairs], jnp.int32)
        pair = jnp.where(jnp.any(targets == me), got, pair)
        have *= 2
    return pair[0], pair[1]


def diag_to_first_pcols(tile0, prows, pcols):
    me = lax.axis_index("prow")
    got = [tile0]
    for d in range(1, prows):
        pairs = []
        for q in range(PANELS):
            pairs.append((q, d * pcols + q))
            pairs.append((pcols + q, ((1 + d) % prows) * pcols + q))
        got.append(lax.ppermute(tile0, ("prow", "pcol"), pairs))
    stack = jnp.stack(got)
    return stack[me], stack[(me + prows - 1) % prows]


def pcol_tree_rounds(pcols):
    zs = pcols // 4

    def idx(x, z, core):
        return (x * zs + z % zs) * 2 + core

    rounds = []
    a_have = [(0, 0)]
    b_have = [(0, 0)]
    steps_a = [("x", 0), ("z", zs // 2)]
    steps_b = [("z", zs // 2), ("x", 0)]
    s = zs // 4
    while s >= 1:
        steps_a.append(("z", s))
        steps_b.append(("z", -s))
        s //= 2
    for (ka, da), (kb, db) in zip(steps_a, steps_b):
        pairs = []
        new_a = []
        for x, z in a_have:
            t = (1 - x, z) if ka == "x" else (x, (z + da) % zs)
            pairs.append((idx(x, z, 0), idx(t[0], t[1], 0)))
            new_a.append(t)
        new_b = []
        for x, z in b_have:
            t = (1 - x, z) if kb == "x" else (x, (z + db) % zs)
            pairs.append((idx(x, z, 1), idx(t[0], t[1], 1)))
            new_b.append(t)
        a_have += new_a
        b_have += new_b
        rounds.append(pairs)
    return rounds


def pcol_broadcast_pair(buf, pcols):
    me = lax.axis_index("pcol")
    for pairs in pcol_tree_rounds(pcols):
        got = lax.ppermute(buf, "pcol", pairs)
        targets = jnp.array([t for _, t in pairs], jnp.int32)
        hit = jnp.any(targets == me)
        buf = jnp.where(hit, got, buf)
    other = lax.ppermute(buf, "pcol", [(i, i ^ 1) for i in range(pcols)])
    core0 = (me % 2) == 0
    return jnp.where(core0, buf, other), jnp.where(core0, other, buf)


def lower_inverse(factor):
    h = factor.shape[0] // 2
    eye = jnp.eye(h, dtype=factor.dtype)
    top = jax.scipy.linalg.solve_triangular(factor[:h, :h], eye, lower=True)
    bottom = jax.scipy.linalg.solve_triangular(factor[h:, h:], eye, lower=True)
    low = -jnp.dot(bottom, jnp.dot(factor[h:, :h], top, precision=HI), precision=HI)
    zero = jnp.zeros_like(eye)
    return jnp.concatenate(
        [jnp.concatenate([top, zero], axis=1), jnp.concatenate([low, bottom], axis=1)], axis=0
    )


def per_device(covariance):
    prows = lax.axis_size("prow")
    pcols = lax.axis_size("pcol")
    p = lax.axis_index("prow")
    q = lax.axis_index("pcol")
    rt = covariance.shape[1]
    tile = covariance.shape[2]
    ct = covariance.shape[4]
    tiles = covariance.reshape(rt, tile, ct, tile)

    first, second = diag_to_first_pcols(tiles[0, :, 0, :], prows, pcols)
    diag_a, diag_b = pcol_broadcast_pair(jnp.stack([first, second]), pcols)

    t0, t1 = prow_from_first_two(tiles[0], prows)

    a00, a10 = diag_a[0], diag_a[1]
    a11 = diag_b[1]
    eye = jnp.eye(tile, dtype=a00.dtype)
    l00 = jnp.tril(jnp.linalg.cholesky(a00))

    col0, col1 = pcol_broadcast_pair(tiles[:, :, 0, :], pcols)

    l00_inv = lower_inverse(l00)
    l10 = jnp.dot(a10, l00_inv.T, precision=HI)
    schur = a11 - jnp.dot(l10, l10.T, precision=HI)
    l11 = jnp.tril(jnp.linalg.cholesky(schur))
    l11_inv = lower_inverse(l11)
    low_inv = -jnp.dot(l11_inv, jnp.dot(l10, l00_inv, precision=HI), precision=HI)
    zero = jnp.zeros_like(eye)
    factor = jnp.concatenate(
        [jnp.concatenate([l00, zero], axis=1), jnp.concatenate([l10, l11], axis=1)], axis=0
    )
    inverse = jnp.concatenate(
        [jnp.concatenate([l00_inv, zero], axis=1), jnp.concatenate([low_inv, l11_inv], axis=1)],
        axis=0,
    )

    rows_panel = jnp.concatenate([col0, col1], axis=-1)
    cols_panel = jnp.concatenate(
        [jnp.transpose(t0, (1, 2, 0)), jnp.transpose(t1, (1, 2, 0))], axis=-1
    )
    cols_solved = jnp.einsum("cak,bk->cab", cols_panel, inverse, precision=HI)
    folded = jnp.einsum("mk,cbm->ckb", inverse, cols_solved, precision=HI)
    update = tiles - jnp.einsum("rak,ckb->racb", rows_panel, folded, precision=HI)

    row_index = jnp.arange(rt, dtype=jnp.int32) * prows + p
    col_index = jnp.arange(ct, dtype=jnp.int32) * pcols + q
    trailing = (row_index >= PANELS)[:, None, None, None] & (col_index >= PANELS)[
        None, None, :, None
    ]
    out = jnp.where(trailing, update, 0.0)

    qc = jnp.minimum(q, PANELS - 1)
    pc = jnp.minimum(p, PANELS - 1)
    inverse_rows = lax.dynamic_slice_in_dim(inverse, qc * tile, tile, axis=0)
    panel_vals = jnp.einsum("rak,bk->rab", rows_panel, inverse_rows, precision=HI)
    diag_tile = lax.dynamic_slice(factor, (pc * tile, qc * tile), (tile, tile))
    panel_vals = panel_vals.at[0].set(jnp.where(p < PANELS, diag_tile, panel_vals[0]))
    out = out.at[:, :, 0, :].set(jnp.where(q < PANELS, panel_vals, out[:, :, 0, :]))
    return out.reshape(1, rt, tile, 1, ct, tile)


def solution(mesh):
    return jax.shard_map(
        per_device,
        mesh=mesh,
        in_specs=(P("prow", None, None, "pcol", None, None),),
        out_specs=P("prow", None, None, "pcol", None, None),
        check_vma=False,
    )
```

```python
import jax
import jax.numpy as jnp
from jax import lax
from jax.sharding import PartitionSpec as P

PANELS = 2
HI = lax.Precision.HIGHEST


def prow_from_first_two(x, prows):
    me = lax.axis_index("prow")
    other = lax.ppermute(x, "prow", [(0, 1), (1, 0)])
    pair = jnp.where(me == 0, jnp.stack([x, other]), jnp.stack([other, x]))
    have = 2
    while have < prows:
        step = prows // 2 if have == 2 else have // 2
        span = 2 * step
        pairs = [(i, i + step) for i in range(prows) if i % span < 2 and i + step < prows]
        got = lax.ppermute(pair, "prow", pairs)
        targets = jnp.array([t for _, t in pairs], jnp.int32)
        pair = jnp.where(jnp.any(targets == me), got, pair)
        have *= 2
    return pair[0], pair[1]


def diag_to_first_pcols(tile0, prows, pcols):
    me = lax.axis_index("prow")
    got = [tile0]
    for d in range(1, prows):
        pairs = []
        for q in range(PANELS):
            pairs.append((q, d * pcols + q))
            pairs.append((pcols + q, ((1 + d) % prows) * pcols + q))
        got.append(lax.ppermute(tile0, ("prow", "pcol"), pairs))
    stack = jnp.stack(got)
    return stack[me], stack[(me + prows - 1) % prows]


def pcol_tree_rounds(pcols):
    zs = pcols // 4

    def idx(x, z, core):
        return (x * zs + z % zs) * 2 + core

    rounds = []
    a_have = [(0, 0)]
    b_have = [(0, 0)]
    steps_a = [("x", 0), ("z", zs // 2)]
    steps_b = [("z", zs // 2), ("x", 0)]
    s = zs // 4
    while s >= 1:
        steps_a.append(("z", s))
        steps_b.append(("z", -s))
        s //= 2
    for (ka, da), (kb, db) in zip(steps_a, steps_b):
        pairs = []
        new_a = []
        for x, z in a_have:
            t = (1 - x, z) if ka == "x" else (x, (z + da) % zs)
            pairs.append((idx(x, z, 0), idx(t[0], t[1], 0)))
            new_a.append(t)
        new_b = []
        for x, z in b_have:
            t = (1 - x, z) if kb == "x" else (x, (z + db) % zs)
            pairs.append((idx(x, z, 1), idx(t[0], t[1], 1)))
            new_b.append(t)
        a_have += new_a
        b_have += new_b
        rounds.append(pairs)
    return rounds


def pcol_broadcast_pair(buf, pcols):
    me = lax.axis_index("pcol")
    for pairs in pcol_tree_rounds(pcols):
        got = lax.ppermute(buf, "pcol", pairs)
        targets = jnp.array([t for _, t in pairs], jnp.int32)
        hit = jnp.any(targets == me)
        buf = jnp.where(hit, got, buf)
    other = lax.ppermute(buf, "pcol", [(i, i ^ 1) for i in range(pcols)])
    core0 = (me % 2) == 0
    return jnp.where(core0, buf, other), jnp.where(core0, other, buf)


def per_device(covariance):
    prows = lax.axis_size("prow")
    pcols = lax.axis_size("pcol")
    p = lax.axis_index("prow")
    q = lax.axis_index("pcol")
    rt = covariance.shape[1]
    tile = covariance.shape[2]
    ct = covariance.shape[4]
    tiles = covariance.reshape(rt, tile, ct, tile)

    t0, t1 = prow_from_first_two(tiles[0], prows)
    diag_a, diag_b = pcol_broadcast_pair(jnp.stack([t0[:, 0, :], t1[:, 0, :]]), pcols)

    a00, a10 = diag_a[0], diag_a[1]
    a11 = diag_b[1]
    eye = jnp.eye(tile, dtype=a00.dtype)
    l00 = jnp.tril(jnp.linalg.cholesky(a00))

    col0, col1 = pcol_broadcast_pair(tiles[:, :, 0, :], pcols)

    l00_inv = jax.scipy.linalg.solve_triangular(l00, eye, lower=True)
    l10 = jnp.dot(a10, l00_inv.T, precision=HI)
    schur = a11 - jnp.dot(l10, l10.T, precision=HI)
    l11 = jnp.tril(jnp.linalg.cholesky(schur))
    l11_inv = jax.scipy.linalg.solve_triangular(l11, eye, lower=True)
    low_inv = -jnp.dot(l11_inv, jnp.dot(l10, l00_inv, precision=HI), precision=HI)
    zero = jnp.zeros_like(eye)
    factor = jnp.concatenate(
        [jnp.concatenate([l00, zero], axis=1), jnp.concatenate([l10, l11], axis=1)], axis=0
    )
    inverse = jnp.concatenate(
        [jnp.concatenate([l00_inv, zero], axis=1), jnp.concatenate([low_inv, l11_inv], axis=1)],
        axis=0,
    )

    rows_panel = jnp.concatenate([col0, col1], axis=-1)
    cols_panel = jnp.concatenate(
        [jnp.transpose(t0, (1, 2, 0)), jnp.transpose(t1, (1, 2, 0))], axis=-1
    )
    cols_solved = jnp.einsum("cak,bk->cab", cols_panel, inverse, precision=HI)
    folded = jnp.einsum("mk,cbm->ckb", inverse, cols_solved, precision=HI)
    update = tiles - jnp.einsum("rak,ckb->racb", rows_panel, folded, precision=HI)

    row_index = jnp.arange(rt, dtype=jnp.int32) * prows + p
    col_index = jnp.arange(ct, dtype=jnp.int32) * pcols + q
    trailing = (row_index >= PANELS)[:, None, None, None] & (col_index >= PANELS)[
        None, None, :, None
    ]
    out = jnp.where(trailing, update, 0.0)

    qc = jnp.minimum(q, PANELS - 1)
    pc = jnp.minimum(p, PANELS - 1)
    inverse_rows = lax.dynamic_slice_in_dim(inverse, qc * tile, tile, axis=0)
    panel_vals = jnp.einsum("rak,bk->rab", rows_panel, inverse_rows, precision=HI)
    diag_tile = lax.dynamic_slice(factor, (pc * tile, qc * tile), (tile, tile))
    panel_vals = panel_vals.at[0].set(jnp.where(p < PANELS, diag_tile, panel_vals[0]))
    out = out.at[:, :, 0, :].set(jnp.where(q < PANELS, panel_vals, out[:, :, 0, :]))
    return out.reshape(1, rt, tile, 1, ct, tile)


def solution(mesh):
    return jax.shard_map(
        per_device,
        mesh=mesh,
        in_specs=(P("prow", None, None, "pcol", None, None),),
        out_specs=P("prow", None, None, "pcol", None, None),
        check_vma=False,
    )
```

```python
import jax
import jax.numpy as jnp
from jax import lax
from jax.sharding import PartitionSpec as P

PANELS = 2
HI = lax.Precision.HIGHEST


def prow_from_first_two(x, prows):
    me = lax.axis_index("prow")
    other = lax.ppermute(x, "prow", [(0, 1), (1, 0)])
    pair = jnp.where(me == 0, jnp.stack([x, other]), jnp.stack([other, x]))
    have = 2
    while have < prows:
        step = prows // 2 if have == 2 else have // 2
        span = 2 * step
        pairs = [(i, i + step) for i in range(prows) if i % span < 2 and i + step < prows]
        got = lax.ppermute(pair, "prow", pairs)
        targets = jnp.array([t for _, t in pairs], jnp.int32)
        pair = jnp.where(jnp.any(targets == me), got, pair)
        have *= 2
    return pair[0], pair[1]


def diag_to_first_pcols(tile0, prows, pcols):
    me = lax.axis_index("prow")
    got = [tile0]
    for d in range(1, prows):
        pairs = []
        for q in range(PANELS):
            pairs.append((q, d * pcols + q))
            pairs.append((pcols + q, ((1 + d) % prows) * pcols + q))
        got.append(lax.ppermute(tile0, ("prow", "pcol"), pairs))
    stack = jnp.stack(got)
    return stack[me], stack[(me + prows - 1) % prows]


def pcol_tree_rounds(pcols):
    zs = pcols // 4

    def idx(x, z, core):
        return (x * zs + z % zs) * 2 + core

    rounds = []
    a_have = [(0, 0)]
    b_have = [(0, 0)]
    steps_a = [("x", 0), ("z", zs // 2)]
    steps_b = [("z", zs // 2), ("x", 0)]
    s = zs // 4
    while s >= 1:
        steps_a.append(("z", s))
        steps_b.append(("z", -s))
        s //= 2
    for (ka, da), (kb, db) in zip(steps_a, steps_b):
        pairs = []
        new_a = []
        for x, z in a_have:
            t = (1 - x, z) if ka == "x" else (x, (z + da) % zs)
            pairs.append((idx(x, z, 0), idx(t[0], t[1], 0)))
            new_a.append(t)
        new_b = []
        for x, z in b_have:
            t = (1 - x, z) if kb == "x" else (x, (z + db) % zs)
            pairs.append((idx(x, z, 1), idx(t[0], t[1], 1)))
            new_b.append(t)
        a_have += new_a
        b_have += new_b
        rounds.append(pairs)
    return rounds


def pcol_broadcast_pair(buf, pcols):
    me = lax.axis_index("pcol")
    for pairs in pcol_tree_rounds(pcols):
        got = lax.ppermute(buf, "pcol", pairs)
        targets = jnp.array([t for _, t in pairs], jnp.int32)
        hit = jnp.any(targets == me)
        buf = jnp.where(hit, got, buf)
    other = lax.ppermute(buf, "pcol", [(i, i ^ 1) for i in range(pcols)])
    core0 = (me % 2) == 0
    return jnp.where(core0, buf, other), jnp.where(core0, other, buf)


def per_device(covariance):
    prows = lax.axis_size("prow")
    pcols = lax.axis_size("pcol")
    p = lax.axis_index("prow")
    q = lax.axis_index("pcol")
    rt = covariance.shape[1]
    tile = covariance.shape[2]
    ct = covariance.shape[4]
    tiles = covariance.reshape(rt, tile, ct, tile)

    first, second = diag_to_first_pcols(tiles[0, :, 0, :], prows, pcols)
    diag_a, diag_b = pcol_broadcast_pair(jnp.stack([first, second]), pcols)

    t0, t1 = prow_from_first_two(tiles[0], prows)

    a00, a10 = diag_a[0], diag_a[1]
    a11 = diag_b[1]
    eye = jnp.eye(tile, dtype=a00.dtype)
    l00 = jnp.tril(jnp.linalg.cholesky(a00))

    col0, col1 = pcol_broadcast_pair(tiles[:, :, 0, :], pcols)

    l00_inv = jax.scipy.linalg.solve_triangular(l00, eye, lower=True)
    l10 = jnp.dot(a10, l00_inv.T, precision=HI)
    schur = a11 - jnp.dot(l10, l10.T, precision=HI)
    l11 = jnp.tril(jnp.linalg.cholesky(schur))
    l11_inv = jax.scipy.linalg.solve_triangular(l11, eye, lower=True)
    low_inv = -jnp.dot(l11_inv, jnp.dot(l10, l00_inv, precision=HI), precision=HI)
    zero = jnp.zeros_like(eye)
    factor = jnp.concatenate(
        [jnp.concatenate([l00, zero], axis=1), jnp.concatenate([l10, l11], axis=1)], axis=0
    )
    inverse = jnp.concatenate(
        [jnp.concatenate([l00_inv, zero], axis=1), jnp.concatenate([low_inv, l11_inv], axis=1)],
        axis=0,
    )

    rows_panel = jnp.concatenate([col0, col1], axis=-1)
    cols_panel = jnp.concatenate(
        [jnp.transpose(t0, (1, 2, 0)), jnp.transpose(t1, (1, 2, 0))], axis=-1
    )
    cols_solved = jnp.einsum("cak,bk->cab", cols_panel, inverse, precision=HI)
    folded = jnp.einsum("mk,cbm->ckb", inverse, cols_solved, precision=HI)

    row_index = jnp.arange(rt, dtype=jnp.int32) * prows + p
    col_index = jnp.arange(ct, dtype=jnp.int32) * pcols + q
    trailing = (row_index >= PANELS)[:, None, None, None] & (col_index >= PANELS)[
        None, None, :, None
    ]
    qc = jnp.minimum(q, PANELS - 1)

    def panel_branch(_):
        inverse_rows = lax.dynamic_slice_in_dim(inverse, qc * tile, tile, axis=0)
        solved = jnp.einsum("rak,bk->rab", rows_panel, inverse_rows, precision=HI)
        rest = tiles[:, :, 1:, :] - jnp.einsum(
            "rak,ckb->racb", rows_panel, folded[1:], precision=HI
        )
        return jnp.concatenate([solved[:, :, None, :], rest], axis=2)

    def trailing_branch(_):
        return tiles - jnp.einsum("rak,ckb->racb", rows_panel, folded, precision=HI)

    update = lax.cond(q < PANELS, panel_branch, trailing_branch, None)
    out = jnp.where(trailing, update, 0.0)

    pc = jnp.minimum(p, PANELS - 1)
    panel_vals = update[:, :, 0, :]
    diag_tile = lax.dynamic_slice(factor, (pc * tile, qc * tile), (tile, tile))
    panel_vals = panel_vals.at[0].set(jnp.where(p < PANELS, diag_tile, panel_vals[0]))
    out = out.at[:, :, 0, :].set(jnp.where(q < PANELS, panel_vals, out[:, :, 0, :]))
    return out.reshape(1, rt, tile, 1, ct, tile)


def solution(mesh):
    return jax.shard_map(
        per_device,
        mesh=mesh,
        in_specs=(P("prow", None, None, "pcol", None, None),),
        out_specs=P("prow", None, None, "pcol", None, None),
        check_vma=False,
    )
```
